256 devices in a mesh: view: 4 (over x_hi, core), gz: 16 (over z, x_lo), xy: 4 (over y).
Axes of the slice: x: 4 (x_hi: 2, x_lo: 2; x = x_hi * 2 + x_lo), y: 4, z: 8, core: 2. Of those that a mesh axis runs over, the one named last changes fastest.
Arguments:
- estimate: float32 [256, 128, 512], P('gz', 'xy', 'view'), may hold values from 0.5 to 2
- images: bfloat16 [16, 256, 128, 512], P('view', 'gz', 'xy'), may hold values from 0.25 to 4
- psf_bank: float32 [16, 31], replicated, may hold values from 0.05 to 1
- psf_index: int32 [16, 3], P('view'), may hold values from 0 to 15
- tissue_bounds: int32 [16, 2], P('gz'), may hold values from 0 to 16, as said below
Outputs:
- updated: float32 [256, 128, 512], P('gz', 'xy', 'view')
The draws below stay inside these ranges and needn't reach their ends.
Inputs may be any that keep to these rules, and one draw needn't show every extreme that they name: `tissue_bounds`: row s holds slab s's first tissue plane and one past its last, both counted within the slab's 16 planes; the first is below the second.
All inputs are finite; a program needn't handle non-finite values.
Results may differ from the reference program's by a relative error of at most 0.00035.
Values may be sent and summed in bfloat16 or wider, within the bound.
No kernel may reach another device: no remote copies, remote signals or barrier semaphores. Data moves between devices by JAX's collectives and lax.ppermute only.
A program may use at most 64 MiB of HBM per device.

```python
import math
import jax
import jax.numpy as jnp
from jax import lax

CZ = 16
X = 512
TAPS = 31
PSFS = 16
HALF = 15
VIEWS = 16
SLABS = 16
Z = 256
Y = 128


def draw_tissue_bounds(key, part):
    base = jax.random.fold_in(key, 7)
    key_low, key_high, key_pick = jax.random.split(base, 3)
    lower = jax.random.randint(key_low, (SLABS,), 0, CZ // 2 + 1)
    upper = CZ - jax.random.randint(key_high, (SLABS,), 0, CZ // 2)
    chosen = jax.random.randint(key_pick, (), 0, SLABS)
    slab_ids = jnp.arange(SLABS)
    lower = jnp.where(slab_ids == chosen, 0, lower)
    upper = jnp.where(slab_ids == chosen, CZ, upper)
    return jnp.stack([lower, upper], axis=1).astype(jnp.int32)


def touch_ends(array, key, smallest, top_value):
    shape = array.shape
    place = [jax.random.randint(jax.random.fold_in(key, axis), (), 0, shape[axis]) for axis in range(len(shape))]
    array = array.at[tuple(place)].set(smallest)
    longest = shape.index(max(shape))
    place[longest] = (place[longest] + 1) % shape[longest]
    return array.at[tuple(place)].set(top_value)


def block_scale(own_key, shape, cuts, smallest, largest):
    gain = 1.0
    for dim, blocks in cuts:
        draws = jax.random.uniform(jax.random.fold_in(jax.random.fold_in(own_key, 6), dim), (blocks,), jnp.float32, smallest / len(cuts), largest / len(cuts))
        gain = gain * jnp.repeat(jnp.exp(draws), shape[dim] // blocks).reshape((-1,) + (1,) * (len(shape) - 1 - dim))
    return gain


def setup_inputs(seed: int = 0) -> dict:
    seeds = jax.random.split(jax.random.key(seed), 6)
    estimate = jnp.clip(jnp.exp(math.log(2.0) - 1.3862944 * jax.random.uniform(seeds[0], (Z, Y, X), jnp.float32) ** block_scale(seeds[0], (Z, Y, X), ((0, 16), (1, 4), (2, 4)), -0.2, 0.2)), 0.5, 2.0)
    images = jnp.clip(jnp.exp(math.log(4.0) - 2.7725887 * jax.random.uniform(seeds[1], (VIEWS, Z, Y, X), jnp.float32) ** block_scale(seeds[1], (VIEWS, Z, Y, X), ((0, 4), (1, 16), (2, 4)), -0.2, 0.2)), 0.25, 4.0).astype(jnp.bfloat16)
    psf_bank = jnp.clip(jnp.exp(jax.random.uniform(seeds[2], (PSFS, TAPS), jnp.float32, math.log(0.05), math.log(1.0))), 0.05, 1.0)
    psf_index = touch_ends(jax.random.randint(seeds[3], (VIEWS, 3), 0, PSFS), jax.random.fold_in(seeds[3], 1), 0, PSFS - 1).astype(jnp.int32)
    tissue_bounds = draw_tissue_bounds(jax.random.fold_in(seeds[5], 71), 0)
    return {"estimate": estimate, "images": images, "psf_bank": psf_bank, "psf_index": psf_index, "tissue_bounds": tissue_bounds}


def correlate(values, taps_row, which_axis, out_count):
    weights = taps_row.astype(jnp.float32)
    total = lax.slice_in_dim(values, 0, out_count, axis=which_axis).astype(jnp.float32) * weights[0]
    for offset in range(1, TAPS):
        total = total + lax.slice_in_dim(values, offset, offset + out_count, axis=which_axis).astype(jnp.float32) * weights[offset]
    return total


def pad_axis(values, which_axis):
    widths = [(0, 0)] * values.ndim
    widths[which_axis] = (HALF, HALF)
    return jnp.pad(values, widths)


def make_taps(psf_bank, psf_index):
    picked = psf_bank[psf_index]
    normed = (picked / jnp.sum(picked, axis=-1, keepdims=True)).astype(jnp.bfloat16)
    return lax.optimization_barrier(normed)


def reference(estimate, images, psf_bank, psf_index, tissue_bounds):
    plane_total = estimate.shape[0]
    row_total = estimate.shape[1]
    col_total = estimate.shape[2]
    plane_ids = jnp.arange(plane_total, dtype=jnp.int32)
    slab_of = plane_ids // CZ
    local_ids = plane_ids - slab_of * CZ
    lower = tissue_bounds[:, 0][slab_of]
    upper = tissue_bounds[:, 1][slab_of]
    in_tissue = ((local_ids >= lower) & (local_ids < upper))[:, None, None]
    masked = jnp.where(in_tissue, estimate, jnp.float32(0.0)).astype(jnp.bfloat16)
    all_taps = make_taps(psf_bank, psf_index)

    def view_step(carry, inputs):
        image, view_taps = inputs
        first_pass = correlate(pad_axis(masked, 0), view_taps[0], 0, plane_total).astype(jnp.bfloat16)
        second_pass = correlate(pad_axis(first_pass, 1), view_taps[1], 1, row_total).astype(jnp.bfloat16)
        blurred = correlate(pad_axis(second_pass, 2), view_taps[2], 2, col_total)
        safe = jnp.where(in_tissue, blurred, jnp.float32(1.0))
        ratios = jnp.where(in_tissue, image.astype(jnp.float32) / safe, jnp.float32(0.0)).astype(jnp.bfloat16)
        back_x = correlate(pad_axis(ratios, 2), view_taps[2][::-1], 2, col_total).astype(jnp.bfloat16)
        back_y = correlate(pad_axis(back_x, 1), view_taps[1][::-1], 1, row_total).astype(jnp.bfloat16)
        back_z = correlate(pad_axis(back_y, 0), view_taps[0][::-1], 0, plane_total)
        return carry + back_z, None

    start = jnp.zeros(estimate.shape, jnp.float32)
    correction, unused = lax.scan(view_step, start, (images, all_taps))
    return jnp.where(in_tissue, estimate * correction / VIEWS, jnp.float32(0.0))
```

```python
import jax
import jax.numpy as jnp
from jax import lax
from jax.sharding import PartitionSpec as P

TAPS = 31
PSFS = 16
HALF = 15


def shift_pairs(axis):
    count = lax.axis_size(axis)
    forward = [(i, i + 1) for i in range(count - 1)]
    backward = [(target, source) for source, target in forward]
    return forward, backward


def padded_2(block, sides, width):
    for axis, dim in sides:
        forward, backward = shift_pairs(axis)
        low = lax.ppermute(
            lax.slice_in_dim(block, block.shape[dim] - width, None, axis=dim), axis, forward
        )
        high = lax.ppermute(lax.slice_in_dim(block, 0, width, axis=dim), axis, backward)
        block = jnp.concatenate([low, block, high], axis=dim)
    return block


def view_taps(psf_bank, psf_index):
    picks = (psf_index[..., None] == jnp.arange(PSFS, dtype=jnp.int32)).astype(jnp.float32)
    picked = jnp.einsum("vap,pt->vat", picks, psf_bank, precision=lax.Precision.HIGHEST)
    normed = (picked / jnp.sum(picked, axis=-1, keepdims=True)).astype(jnp.bfloat16)
    return lax.optimization_barrier(normed)


def bands(taps, in_count, out_count):
    window_ids = jnp.arange(in_count, dtype=jnp.int32)[:, None]
    output_ids = jnp.arange(out_count, dtype=jnp.int32)[None, :]
    offsets = window_ids - output_ids
    onehot = offsets[..., None] == jnp.arange(TAPS, dtype=jnp.int32)
    band = jnp.sum(
        jnp.where(onehot[None], taps.astype(jnp.float32)[:, None, None, :], 0.0), axis=-1
    )
    return band.astype(jnp.bfloat16)


def x_bands(taps, col_total):
    block = 128
    window = lax.optimization_barrier(bands(taps, block + 2 * HALF, block))
    padded = jnp.pad(window, ((0, 0), (col_total, col_total), (0, 0)))
    parts = []
    for c in range(col_total // block):
        start = col_total - block * c + HALF
        parts.append(lax.slice_in_dim(padded, start, start + col_total, axis=1))
    return jnp.concatenate(parts, axis=2)


def on_device(estimate, images, psf_bank, psf_index, tissue_bounds):
    plane_count = estimate.shape[0]
    row_count = estimate.shape[1]
    view_count = images.shape[0]
    col_total = images.shape[-1]
    planes = jnp.arange(plane_count, dtype=jnp.int32)
    in_tissue = ((planes >= tissue_bounds[0, 0]) & (planes < tissue_bounds[0, 1]))[:, None, None]
    masked = jnp.where(in_tissue, estimate, 0.0).astype(jnp.bfloat16)
    all_taps = view_taps(psf_bank, psf_index)
    z_taps = all_taps[:, 0]
    y_taps = all_taps[:, 1]
    x_taps = all_taps[:, 2]
    whole_rows = lax.all_gather(masked, "view", axis=2, tiled=True)
    framed = padded_2(whole_rows, (("gz", 0), ("xy", 1)), HALF)

    z_band = bands(z_taps, plane_count + 2 * HALF, plane_count)
    y_band = bands(y_taps, row_count + 2 * HALF, row_count)
    x_band = x_bands(x_taps, col_total)
    first = jnp.einsum(
        "vwo,wyx->voyx", z_band, framed, preferred_element_type=jnp.float32
    ).astype(jnp.bfloat16)
    second = jnp.einsum(
        "vzwx,vwo->vzox", first, y_band, preferred_element_type=jnp.float32
    ).astype(jnp.bfloat16)
    blurred = jnp.einsum("vzyw,vwo->vzyo", second, x_band, preferred_element_type=jnp.float32)
    safe = jnp.where(in_tissue[None], blurred, 1.0)
    ratios = jnp.where(in_tissue[None], images.astype(jnp.float32) / safe, 0.0).astype(
        jnp.bfloat16
    )
    back_x = jnp.einsum(
        "vzyw,vow->vzyo", ratios, x_band, preferred_element_type=jnp.float32
    ).astype(jnp.bfloat16)

    rows_framed = padded_2(back_x, (("xy", 2),), HALF)
    back_y_band = bands(y_taps[:, ::-1], row_count + 2 * HALF, row_count)
    back_y = jnp.einsum(
        "vzwx,vwo->vzox", rows_framed, back_y_band, preferred_element_type=jnp.float32
    ).astype(jnp.bfloat16)

    spread = jnp.einsum("vop,vpyx->oyx", z_band, back_y, preferred_element_type=jnp.float32)
    forward, backward = shift_pairs("gz")
    from_prev = lax.ppermute(spread[plane_count + HALF :], "gz", forward)
    from_next = lax.ppermute(spread[:HALF], "gz", backward)
    own = spread[HALF : plane_count + HALF]
    extra = plane_count - HALF
    correction = (
        own
        + jnp.pad(from_prev, ((0, extra), (0, 0), (0, 0)))
        + jnp.pad(from_next, ((extra, 0), (0, 0), (0, 0)))
    )
    owned = lax.psum_scatter(correction, "view", scatter_dimension=2, tiled=True)
    total_views = view_count * lax.axis_size("view")
    return jnp.where(in_tissue, estimate * owned / total_views, 0.0)


def solution(mesh):
    placed = (
        P("gz", "xy", "view"),
        P("view", "gz", "xy", None),
        P(),
        P("view", None),
        P("gz", None),
    )
    return jax.shard_map(
        on_device, mesh=mesh, in_specs=placed, out_specs=P("gz", "xy", "view"), check_vma=False
    )
```

```python
import jax
import jax.numpy as jnp
from jax import lax
from jax.sharding import PartitionSpec as P

TAPS = 31
PSFS = 16
HALF = 15


def shift_pairs(axis):
    count = lax.axis_size(axis)
    forward = [(i, i + 1) for i in range(count - 1)]
    backward = [(target, source) for source, target in forward]
    return forward, backward


def padded_2(block, sides, width):
    for axis, dim in sides:
        forward, backward = shift_pairs(axis)
        low = lax.ppermute(
            lax.slice_in_dim(block, block.shape[dim] - width, None, axis=dim), axis, forward
        )
        high = lax.ppermute(lax.slice_in_dim(block, 0, width, axis=dim), axis, backward)
        block = jnp.concatenate([low, block, high], axis=dim)
    return block


def view_taps(psf_bank, psf_index):
    picks = (psf_index[..., None] == jnp.arange(PSFS, dtype=jnp.int32)).astype(jnp.float32)
    picked = jnp.einsum("vap,pt->vat", picks, psf_bank, precision=lax.Precision.HIGHEST)
    normed = (picked / jnp.sum(picked, axis=-1, keepdims=True)).astype(jnp.bfloat16)
    return lax.optimization_barrier(normed)


def bands(taps, in_count, out_count):
    window_ids = jnp.arange(in_count, dtype=jnp.int32)[:, None]
    output_ids = jnp.arange(out_count, dtype=jnp.int32)[None, :]
    offsets = window_ids - output_ids
    onehot = offsets[..., None] == jnp.arange(TAPS, dtype=jnp.int32)
    band = jnp.sum(
        jnp.where(onehot[None], taps.astype(jnp.float32)[:, None, None, :], 0.0), axis=-1
    )
    return band.astype(jnp.bfloat16)


def x_bands(taps, col_total):
    block = 128
    window = lax.optimization_barrier(bands(taps, block + 2 * HALF, block))
    padded = jnp.pad(window, ((0, 0), (col_total, col_total), (0, 0)))
    parts = []
    for c in range(col_total // block):
        start = col_total - block * c + HALF
        parts.append(lax.slice_in_dim(padded, start, start + col_total, axis=1))
    return jnp.concatenate(parts, axis=2)


def on_device(estimate, images, psf_bank, psf_index, tissue_bounds):
    plane_count = estimate.shape[0]
    row_count = estimate.shape[1]
    view_count = images.shape[0]
    col_total = images.shape[-1]
    planes = jnp.arange(plane_count, dtype=jnp.int32)
    in_tissue = ((planes >= tissue_bounds[0, 0]) & (planes < tissue_bounds[0, 1]))[:, None, None]
    masked = jnp.where(in_tissue, estimate, 0.0).astype(jnp.bfloat16)
    all_taps = view_taps(psf_bank, psf_index)
    z_taps = all_taps[:, 0]
    y_taps = all_taps[:, 1]
    x_taps = all_taps[:, 2]
    whole_rows = lax.all_gather(masked, "view", axis=2, tiled=True)
    framed = padded_2(whole_rows, (("gz", 0), ("xy", 1)), HALF)

    z_band = bands(z_taps, plane_count + 2 * HALF, plane_count)
    y_band = bands(y_taps, row_count + 2 * HALF, row_count)
    x_band = x_bands(x_taps, col_total)
    first = jnp.einsum(
        "vwo,wyx->voyx", z_band, framed, preferred_element_type=jnp.float32
    ).astype(jnp.bfloat16)
    second = jnp.einsum(
        "vzwx,vwo->vzox", first, y_band, preferred_element_type=jnp.float32
    ).astype(jnp.bfloat16)
    blurred = jnp.einsum("vzyw,vwo->vzyo", second, x_band, preferred_element_type=jnp.float32)
    safe = jnp.where(in_tissue[None], blurred, 1.0)
    ratios = jnp.where(in_tissue[None], images.astype(jnp.float32) / safe, 0.0).astype(
        jnp.bfloat16
    )
    back_x = jnp.einsum(
        "vzyw,vow->vzyo", ratios, x_band, preferred_element_type=jnp.float32
    ).astype(jnp.bfloat16)

    rows_framed = padded_2(back_x, (("xy", 2),), HALF)
    back_y_band = bands(y_taps[:, ::-1], row_count + 2 * HALF, row_count)
    back_y = jnp.einsum(
        "vzwx,vwo->vzox", rows_framed, back_y_band, preferred_element_type=jnp.float32
    ).astype(jnp.bfloat16)

    spread = jnp.einsum("vop,vpyx->oyx", z_band, back_y, preferred_element_type=jnp.float32)
    col_block = col_total // lax.axis_size("view")
    position = lax.axis_index("view")
    core = position % 2
    half = position // 2
    core_pairs = [(i, i ^ 1) for i in range(lax.axis_size("view"))]
    far_pairs = [(i, i ^ 2) for i in range(lax.axis_size("view"))]

    def pick(values, first):
        return jnp.concatenate(
            [
                lax.dynamic_slice_in_dim(values, col_block * first, col_block, axis=2),
                lax.dynamic_slice_in_dim(values, col_block * (first + 2), col_block, axis=2),
            ],
            axis=2,
        )

    spread = pick(spread, core) + lax.ppermute(pick(spread, 1 - core), "view", core_pairs)
    forward, backward = shift_pairs("gz")
    from_prev = lax.ppermute(spread[plane_count + HALF :], "gz", forward)
    from_next = lax.ppermute(spread[:HALF], "gz", backward)
    own = spread[HALF : plane_count + HALF]
    extra = plane_count - HALF
    correction = (
        own
        + jnp.pad(from_prev, ((0, extra), (0, 0), (0, 0)))
        + jnp.pad(from_next, ((extra, 0), (0, 0), (0, 0)))
    )
    owned = lax.dynamic_slice_in_dim(correction, col_block * half, col_block, axis=2)
    sent = lax.dynamic_slice_in_dim(correction, col_block * (1 - half), col_block, axis=2)
    owned = owned + lax.ppermute(sent, "view", far_pairs)
    total_views = view_count * lax.axis_size("view")
    return jnp.where(in_tissue, estimate * owned / total_views, 0.0)


def solution(mesh):
    placed = (
        P("gz", "xy", "view"),
        P("view", "gz", "xy", None),
        P(),
        P("view", None),
        P("gz", None),
    )
    return jax.shard_map(
        on_device, mesh=mesh, in_specs=placed, out_specs=P("gz", "xy", "view"), check_vma=False
    )
```

```python
import jax
import jax.numpy as jnp
from jax import lax
from jax.sharding import PartitionSpec as P

TAPS = 31
PSFS = 16
HALF = 15


def shift_pairs(axis):
    count = lax.axis_size(axis)
    forward = [(i, i + 1) for i in range(count - 1)]
    backward = [(target, source) for source, target in forward]
    return forward, backward


def padded_2(block, sides, width):
    for axis, dim in sides:
        forward, backward = shift_pairs(axis)
        low = lax.ppermute(
            lax.slice_in_dim(block, block.shape[dim] - width, None, axis=dim), axis, forward
        )
        high = lax.ppermute(lax.slice_in_dim(block, 0, width, axis=dim), axis, backward)
        block = jnp.concatenate([low, block, high], axis=dim)
    return block


def view_taps(psf_bank, psf_index):
    picks = (psf_index[..., None] == jnp.arange(PSFS, dtype=jnp.int32)).astype(jnp.float32)
    picked = jnp.einsum("vap,pt->vat", picks, psf_bank, precision=lax.Precision.HIGHEST)
    normed = (picked / jnp.sum(picked, axis=-1, keepdims=True)).astype(jnp.bfloat16)
    return lax.optimization_barrier(normed)


def bands(taps, in_count, out_count):
    window_ids = jnp.arange(in_count, dtype=jnp.int32)[:, None]
    output_ids = jnp.arange(out_count, dtype=jnp.int32)[None, :]
    offsets = window_ids - output_ids
    onehot = offsets[..., None] == jnp.arange(TAPS, dtype=jnp.int32)
    band = jnp.sum(
        jnp.where(onehot[None], taps.astype(jnp.float32)[:, None, None, :], 0.0), axis=-1
    )
    return band.astype(jnp.bfloat16)


def x_bands(taps, col_total):
    block = 128
    window = lax.optimization_barrier(bands(taps, block + 2 * HALF, block))
    padded = jnp.pad(window, ((0, 0), (col_total, col_total), (0, 0)))
    parts = []
    for c in range(col_total // block):
        start = col_total - block * c + HALF
        parts.append(lax.slice_in_dim(padded, start, start + col_total, axis=1))
    return jnp.concatenate(parts, axis=2)


def on_device(estimate, images, psf_bank, psf_index, tissue_bounds):
    plane_count = estimate.shape[0]
    row_count = estimate.shape[1]
    view_count = images.shape[0]
    col_total = images.shape[-1]
    planes = jnp.arange(plane_count, dtype=jnp.int32)
    in_tissue = ((planes >= tissue_bounds[0, 0]) & (planes < tissue_bounds[0, 1]))[:, None, None]
    masked = jnp.where(in_tissue, estimate, 0.0).astype(jnp.bfloat16)
    all_taps = view_taps(psf_bank, psf_index)
    z_taps = all_taps[:, 0]
    y_taps = all_taps[:, 1]
    x_taps = all_taps[:, 2]
    whole_rows = lax.all_gather(masked, "view", axis=2, tiled=True)
    framed = padded_2(whole_rows, (("gz", 0), ("xy", 1)), HALF)

    z_band = bands(z_taps, plane_count + 2 * HALF, plane_count)
    y_band = bands(y_taps, row_count + 2 * HALF, row_count)
    back_y_band = bands(y_taps[:, ::-1], row_count + 2 * HALF, row_count)
    x_band = x_bands(x_taps, col_total)

    col_block = col_total // lax.axis_size("view")
    position = lax.axis_index("view")
    core = position % 2
    half = position // 2
    core_pairs = [(i, i ^ 1) for i in range(lax.axis_size("view"))]
    far_pairs = [(i, i ^ 2) for i in range(lax.axis_size("view"))]
    forward, backward = shift_pairs("gz")
    extra = plane_count - HALF

    def pick(values, first):
        return jnp.concatenate(
            [
                lax.dynamic_slice_in_dim(values, col_block * first, col_block, axis=2),
                lax.dynamic_slice_in_dim(values, col_block * (first + 2), col_block, axis=2),
            ],
            axis=2,
        )

    def group_correction(views):
        first = jnp.einsum(
            "vwo,wyx->voyx", z_band[views], framed, preferred_element_type=jnp.float32
        ).astype(jnp.bfloat16)
        second = jnp.einsum(
            "vzwx,vwo->vzox", first, y_band[views], preferred_element_type=jnp.float32
        ).astype(jnp.bfloat16)
        blurred = jnp.einsum(
            "vzyw,vwo->vzyo", second, x_band[views], preferred_element_type=jnp.float32
        )
        safe = jnp.where(in_tissue[None], blurred, 1.0)
        ratios = jnp.where(
            in_tissue[None], images[views].astype(jnp.float32) / safe, 0.0
        ).astype(jnp.bfloat16)
        back_x = jnp.einsum(
            "vzyw,vow->vzyo", ratios, x_band[views], preferred_element_type=jnp.float32
        ).astype(jnp.bfloat16)
        rows_framed = padded_2(back_x, (("xy", 2),), HALF)
        back_y = jnp.einsum(
            "vzwx,vwo->vzox", rows_framed, back_y_band[views], preferred_element_type=jnp.float32
        ).astype(jnp.bfloat16)
        spread = jnp.einsum(
            "vop,vpyx->oyx", z_band[views], back_y, preferred_element_type=jnp.float32
        )
        spread = pick(spread, core) + lax.ppermute(pick(spread, 1 - core), "view", core_pairs)
        from_prev = lax.ppermute(spread[plane_count + HALF :], "gz", forward)
        from_next = lax.ppermute(spread[:HALF], "gz", backward)
        return (
            spread[HALF : plane_count + HALF]
            + jnp.pad(from_prev, ((0, extra), (0, 0), (0, 0)))
            + jnp.pad(from_next, ((extra, 0), (0, 0), (0, 0)))
        )

    groups = 2
    per_group = view_count // groups
    correction = group_correction(slice(0, per_group))
    for g in range(1, groups):
        correction = correction + group_correction(slice(g * per_group, (g + 1) * per_group))
    owned = lax.dynamic_slice_in_dim(correction, col_block * half, col_block, axis=2)
    sent = lax.dynamic_slice_in_dim(correction, col_block * (1 - half), col_block, axis=2)
    owned = owned + lax.ppermute(sent, "view", far_pairs)
    total_views = view_count * lax.axis_size("view")
    return jnp.where(in_tissue, estimate * owned / total_views, 0.0)


def solution(mesh):
    placed = (
        P("gz", "xy", "view"),
        P("view", "gz", "xy", None),
        P(),
        P("view", None),
        P("gz", None),
    )
    return jax.shard_map(
        on_device, mesh=mesh, in_specs=placed, out_specs=P("gz", "xy", "view"), check_vma=False
    )
```

```python
import jax
import numpy as np
import jax.numpy as jnp
from jax import lax
from jax.sharding import PartitionSpec as P

TAPS = 31
PSFS = 16
HALF = 15


def shift_pairs(axis):
    count = lax.axis_size(axis)
    forward = [(i, i + 1) for i in range(count - 1)]
    backward = [(target, source) for source, target in forward]
    return forward, backward


def shifted(block, axes, deltas):
    sizes = [lax.axis_size(a) for a in axes]
    pairs = []
    for flat in range(int(np.prod(sizes))):
        coords = list(np.unravel_index(flat, sizes))
        target = [c + d for c, d in zip(coords, deltas)]
        if all(0 <= t < n for t, n in zip(target, sizes)):
            pairs.append((flat, int(np.ravel_multi_index(target, sizes))))
    return lax.ppermute(block, tuple(axes), pairs)


def framed_zy(block, width):
    ax = ("gz", "xy")
    low_z = block[block.shape[0] - width :]
    high_z = block[:width]
    top = jnp.concatenate(
        [
            shifted(low_z[:, low_z.shape[1] - width :], ax, (1, 1)),
            shifted(low_z, ("gz",), (1,)),
            shifted(low_z[:, :width], ax, (1, -1)),
        ],
        axis=1,
    )
    middle = jnp.concatenate(
        [
            shifted(block[:, block.shape[1] - width :], ("xy",), (1,)),
            block,
            shifted(block[:, :width], ("xy",), (-1,)),
        ],
        axis=1,
    )
    bottom = jnp.concatenate(
        [
            shifted(high_z[:, high_z.shape[1] - width :], ax, (-1, 1)),
            shifted(high_z, ("gz",), (-1,)),
            shifted(high_z[:, :width], ax, (-1, -1)),
        ],
        axis=1,
    )
    return jnp.concatenate([top, middle, bottom], axis=0)


def padded_2(block, sides, width):
    for axis, dim in sides:
        forward, backward = shift_pairs(axis)
        low = lax.ppermute(
            lax.slice_in_dim(block, block.shape[dim] - width, None, axis=dim), axis, forward
        )
        high = lax.ppermute(lax.slice_in_dim(block, 0, width, axis=dim), axis, backward)
        block = jnp.concatenate([low, block, high], axis=dim)
    return block


def view_taps(psf_bank, psf_index):
    picks = (psf_index[..., None] == jnp.arange(PSFS, dtype=jnp.int32)).astype(jnp.float32)
    picked = jnp.einsum("vap,pt->vat", picks, psf_bank, precision=lax.Precision.HIGHEST)
    normed = (picked / jnp.sum(picked, axis=-1, keepdims=True)).astype(jnp.bfloat16)
    return lax.optimization_barrier(normed)


def bands(taps, in_count, out_count):
    window_ids = jnp.arange(in_count, dtype=jnp.int32)[:, None]
    output_ids = jnp.arange(out_count, dtype=jnp.int32)[None, :]
    offsets = window_ids - output_ids
    onehot = offsets[..., None] == jnp.arange(TAPS, dtype=jnp.int32)
    band = jnp.sum(
        jnp.where(onehot[None], taps.astype(jnp.float32)[:, None, None, :], 0.0), axis=-1
    )
    return band.astype(jnp.bfloat16)


def x_bands(taps, col_total):
    block = 128
    window = lax.optimization_barrier(bands(taps, block + 2 * HALF, block))
    padded = jnp.pad(window, ((0, 0), (col_total, col_total), (0, 0)))
    parts = []
    for c in range(col_total // block):
        start = col_total - block * c + HALF
        parts.append(lax.slice_in_dim(padded, start, start + col_total, axis=1))
    return jnp.concatenate(parts, axis=2)


def on_device(estimate, images, psf_bank, psf_index, tissue_bounds):
    plane_count = estimate.shape[0]
    row_count = estimate.shape[1]
    view_count = images.shape[0]
    col_total = images.shape[-1]
    planes = jnp.arange(plane_count, dtype=jnp.int32)
    in_tissue = ((planes >= tissue_bounds[0, 0]) & (planes < tissue_bounds[0, 1]))[:, None, None]
    masked = jnp.where(in_tissue, estimate, 0.0).astype(jnp.bfloat16)
    all_taps = view_taps(psf_bank, psf_index)
    z_taps = all_taps[:, 0]
    y_taps = all_taps[:, 1]
    x_taps = all_taps[:, 2]
    whole_rows = lax.all_gather(masked, "view", axis=2, tiled=True)
    framed = framed_zy(whole_rows, HALF)

    z_band = bands(z_taps, plane_count + 2 * HALF, plane_count)
    y_band = bands(y_taps, row_count + 2 * HALF, row_count)
    x_band = x_bands(x_taps, col_total)
    first = jnp.einsum(
        "vwo,wyx->voyx", z_band, framed, preferred_element_type=jnp.float32
    ).astype(jnp.bfloat16)
    second = jnp.einsum(
        "vzwx,vwo->vzox", first, y_band, preferred_element_type=jnp.float32
    ).astype(jnp.bfloat16)
    blurred = jnp.einsum("vzyw,vwo->vzyo", second, x_band, preferred_element_type=jnp.float32)
    safe = jnp.where(in_tissue[None], blurred, 1.0)
    ratios = jnp.where(in_tissue[None], images.astype(jnp.float32) / safe, 0.0).astype(
        jnp.bfloat16
    )
    back_x = jnp.einsum(
        "vzyw,vow->vzyo", ratios, x_band, preferred_element_type=jnp.float32
    ).astype(jnp.bfloat16)

    rows_framed = padded_2(back_x, (("xy", 2),), HALF)
    back_y_band = bands(y_taps[:, ::-1], row_count + 2 * HALF, row_count)
    back_y = jnp.einsum(
        "vzwx,vwo->vzox", rows_framed, back_y_band, preferred_element_type=jnp.float32
    ).astype(jnp.bfloat16)

    spread = jnp.einsum("vop,vpyx->oyx", z_band, back_y, preferred_element_type=jnp.float32)
    col_block = col_total // lax.axis_size("view")
    position = lax.axis_index("view")
    core = position % 2
    half = position // 2
    core_pairs = [(i, i ^ 1) for i in range(lax.axis_size("view"))]
    far_pairs = [(i, i ^ 2) for i in range(lax.axis_size("view"))]

    def pick(values, first):
        return jnp.concatenate(
            [
                lax.dynamic_slice_in_dim(values, col_block * first, col_block, axis=2),
                lax.dynamic_slice_in_dim(values, col_block * (first + 2), col_block, axis=2),
            ],
            axis=2,
        )

    spread = pick(spread, core) + lax.ppermute(pick(spread, 1 - core), "view", core_pairs)
    mine = lax.dynamic_slice_in_dim(spread, col_block * half, col_block, axis=2)
    theirs = lax.dynamic_slice_in_dim(spread, col_block * (1 - half), col_block, axis=2)
    extra = plane_count - HALF
    far = lax.axis_size("view") // 2
    edges = (
        shifted(mine[plane_count + HALF :], ("gz",), (1,))
        + shifted(theirs[plane_count + HALF :], ("view", "gz"), (far, 1))
        + shifted(theirs[plane_count + HALF :], ("view", "gz"), (-far, 1))
    )
    edges_next = (
        shifted(mine[:HALF], ("gz",), (-1,))
        + shifted(theirs[:HALF], ("view", "gz"), (far, -1))
        + shifted(theirs[:HALF], ("view", "gz"), (-far, -1))
    )
    owned = (
        mine[HALF : plane_count + HALF]
        + lax.ppermute(theirs[HALF : plane_count + HALF], "view", far_pairs)
        + jnp.pad(edges, ((0, extra), (0, 0), (0, 0)))
        + jnp.pad(edges_next, ((extra, 0), (0, 0), (0, 0)))
    )
    total_views = view_count * lax.axis_size("view")
    return jnp.where(in_tissue, estimate * owned / total_views, 0.0)


def solution(mesh):
    placed = (
        P("gz", "xy", "view"),
        P("view", "gz", "xy", None),
        P(),
        P("view", None),
        P("gz", None),
    )
    return jax.shard_map(
        on_device, mesh=mesh, in_specs=placed, out_specs=P("gz", "xy", "view"), check_vma=False
    )
```
